32 devices in a mesh: section: 2 (over x), dp: 4 (over z), mp: 4 (over y, core).
Axes of the slice: x: 2, y: 2, z: 4, core: 2. Of those that a mesh axis runs over, the one named last changes fastest.
Arguments:
- queries: bfloat16 [2, 4, 640, 4096], P('section', 'dp', None, 'mp')
- keys: bfloat16 [2, 4, 640, 4096], P('section', 'dp', None, 'mp')
- values: bfloat16 [2, 4, 640, 4096], P('section', 'dp', None, 'mp'), may hold values from -6 to 6
- grad_out: bfloat16 [2, 4, 640, 4096], P('section', 'dp', None, 'mp'), may hold values from -6 to 6
- positions: int32 [2, 4, 640], P('section', 'dp'), may hold values from 0 to 319, as said below
Outputs:
- received: bfloat16 [2, 4, 3, 640, 4096], P('section', 'dp', None, 'mp')
- bias_grad: float32 [2, 3, 4096], P('section')
The draws below stay inside these ranges and needn't reach their ends.
Inputs may be any that keep to these rules, and one draw needn't show every extreme that they name: `positions`: along each sequence a position is 0 or one more than the position before it; the first is 0; a document starts at token 320, and none is longer than 320 tokens.
All inputs are finite; a program needn't handle non-finite values.
Results may differ from the reference program's by a relative error of at most 0.0065.
Values may be sent and summed in bfloat16 or wider, within the bound.
No kernel may reach another device: no remote copies, remote signals or barrier semaphores. Data moves between devices by JAX's collectives and lax.ppermute only.
A program may use at most 64 MiB of HBM per device.

```python
import math
import jax
import jax.numpy as jnp
from jax import lax

HEADS = 32
HEAD_DIM = 128
LEN = 640
HD = 4096
SECTIONS = 2
REPLICAS = 4


def paired_draw(key):
    base = jax.random.fold_in(key, 17)
    first, second = jax.random.split(base, 2)
    shape = (SECTIONS, REPLICAS, LEN, HEADS * HEAD_DIM)
    query_draw = jax.random.truncated_normal(first, -6.0, 6.0, shape, jnp.float32)
    key_draw = jax.random.truncated_normal(second, -6.0, 6.0, shape, jnp.float32)
    return (query_draw, key_draw)


def draw_queries(key, part):
    return paired_draw(key)[0].astype(jnp.bfloat16)


def draw_keys(key, part):
    return paired_draw(key)[1].astype(jnp.bfloat16)


def draw_positions(key, part):
    base = jax.random.fold_in(key, 29)
    shape = (SECTIONS, REPLICAS, LEN)
    half = LEN // 2
    indices = jnp.broadcast_to(jnp.arange(LEN, dtype=jnp.int32), shape)
    marks = (jax.random.randint(base, shape, 0, LEN) < 4) & (indices > half)
    marks = marks | (indices == 0) | (indices == half)
    starts = jnp.where(marks, indices, 0).astype(jnp.int32)
    return (indices - lax.cummax(starts, axis=2)).astype(jnp.int32)


def levels(rng, shape, cuts, smallest, high):
    def one(dim, blocks):
        heights = jax.random.uniform(jax.random.fold_in(jax.random.fold_in(rng, 6), dim), (blocks,), jnp.float32, smallest / len(cuts), high / len(cuts))
        return jnp.repeat(jnp.exp(heights), shape[dim] // blocks).reshape((-1,) + (1,) * (len(shape) - dim - 1))

    gain = one(*cuts[0])
    for cut in cuts[1:]:
        gain = gain * one(*cut)
    return gain


def scatter_about(own_key, shape, spread, reach, pieces=(), kind=jnp.bfloat16):
    drawn = jax.random.normal(own_key, shape, jnp.float32) * spread
    if len(pieces) > 0:
        drawn = levels(own_key, shape, pieces, -0.22, 0.18) * drawn
    return jnp.clip(drawn, min=-reach, max=reach).astype(kind)


def setup_inputs(seed: int = 0) -> dict:
    streams_of = jax.random.split(jax.random.key(seed), 6)
    queries = draw_queries(jax.random.fold_in(streams_of[5], 71), 0)
    keys = draw_keys(jax.random.fold_in(streams_of[5], 71), 0)
    values = scatter_about(streams_of[2], (SECTIONS, REPLICAS, LEN, HD), 1.0, 6.0, ((0, 2), (1, 4), (3, 4)))
    grad_out = scatter_about(streams_of[3], (SECTIONS, REPLICAS, LEN, HD), 1.0, 6.0, ((0, 2), (1, 4), (3, 4)))
    positions = draw_positions(jax.random.fold_in(streams_of[5], 71), 0)
    return dict(queries=queries, keys=keys, values=values, grad_out=grad_out, positions=positions)


def core_grads(query_rows, key_rows, value_rows, grad_rows, token_positions):
    length = query_rows.shape[0]
    scaling = 1.0 / math.sqrt(HEAD_DIM)
    query_heads = query_rows.astype(jnp.float32).reshape(length, HEADS, HEAD_DIM)
    key_heads = key_rows.astype(jnp.float32).reshape(length, HEADS, HEAD_DIM)
    value_heads = value_rows.astype(jnp.float32).reshape(length, HEADS, HEAD_DIM)
    grad_heads = grad_rows.astype(jnp.float32).reshape(length, HEADS, HEAD_DIM)
    indices = jnp.arange(length, dtype=jnp.int32)
    allowed = (indices[None, :] <= indices[:, None]) & (indices[None, :] >= (indices - token_positions)[:, None])
    scores = jnp.einsum('qhd,khd->hqk', query_heads, key_heads) * scaling
    scores = jnp.where(allowed[None], scores, jnp.float32(-1e+30))
    highest = lax.optimization_barrier(jnp.max(scores, axis=-1, keepdims=True))
    expont = jnp.exp(scores - highest)
    attn = expont / lax.optimization_barrier(jnp.sum(expont, axis=-1, keepdims=True))
    attn_low = attn.astype(jnp.bfloat16).astype(jnp.float32)
    grad_v = jnp.einsum('hqk,qhd->khd', attn_low, grad_heads).astype(jnp.bfloat16)
    grad_attn = jnp.einsum('qhd,khd->hqk', grad_heads, value_heads)
    delta = lax.optimization_barrier(jnp.sum(attn * grad_attn, axis=-1, keepdims=True))
    grad_scores = (attn * (grad_attn - delta) * scaling).astype(jnp.bfloat16).astype(jnp.float32)
    grad_q = jnp.einsum('hqk,khd->qhd', grad_scores, key_heads).astype(jnp.bfloat16)
    grad_k = jnp.einsum('hqk,qhd->khd', grad_scores, query_heads).astype(jnp.bfloat16)
    stacked = jnp.stack([grad_q, grad_k, grad_v])
    return stacked.reshape(3, length, HEADS * HEAD_DIM)

def reference(queries, keys, values, grad_out, positions):

    def flatten(array):
        return array.reshape((SECTIONS * REPLICAS,) + array.shape[2:])

    def one_pair(items):
        return core_grads(items[0], items[1], items[2], items[3], items[4])
    sent = lax.map(one_pair, (flatten(queries), flatten(keys), flatten(values), flatten(grad_out), flatten(positions)))
    sent = sent.reshape(SECTIONS, REPLICAS, 3, LEN, HEADS * HEAD_DIM)
    received = jnp.concatenate([sent[1:], jnp.zeros_like(sent[:1])], axis=0)
    totals = lax.optimization_barrier(jnp.sum(received.astype(jnp.float32), axis=(1, 3)))
    bias_grad = totals / math.sqrt(REPLICAS * LEN)
    return (received, bias_grad)
```

```python
import math

import jax
import jax.numpy as jnp
from jax import lax
from jax.sharding import PartitionSpec as P

HEAD_DIM = 128
CHUNK_HEADS = 2


def chunk_grads(query_rows, key_rows, value_rows, grad_rows, allowed, halves):
    length, width = query_rows.shape
    heads = width // HEAD_DIM
    block = length // halves
    scaling = 1.0 / math.sqrt(HEAD_DIM)

    def split(rows):
        return rows.reshape(halves, block, heads, HEAD_DIM)

    q, k, v, g = split(query_rows), split(key_rows), split(value_rows), split(grad_rows)
    scores = jnp.einsum("bqhd,bkhd->bhqk", q, k, preferred_element_type=jnp.float32) * scaling
    scores = jnp.where(allowed[:, None], scores, jnp.float32(-1e30))
    highest = jnp.max(scores, axis=-1, keepdims=True)
    expont = jnp.exp(scores - highest)
    attn = expont / jnp.sum(expont, axis=-1, keepdims=True)
    attn_low = attn.astype(jnp.bfloat16)
    grad_v = jnp.einsum("bhqk,bqhd->bkhd", attn_low, g, preferred_element_type=jnp.float32)
    grad_attn = jnp.einsum("bqhd,bkhd->bhqk", g, v, preferred_element_type=jnp.float32)
    delta = jnp.sum(attn * grad_attn, axis=-1, keepdims=True)
    grad_scores = (attn * (grad_attn - delta) * scaling).astype(jnp.bfloat16)
    grad_q = jnp.einsum("bhqk,bkhd->bqhd", grad_scores, k, preferred_element_type=jnp.float32)
    grad_k = jnp.einsum("bhqk,bqhd->bkhd", grad_scores, q, preferred_element_type=jnp.float32)
    blocks = jnp.stack([grad_q, grad_k, grad_v]).astype(jnp.bfloat16)
    return blocks.reshape(3, length, width)


def per_device(queries, keys, values, grad_out, positions):
    query_rows = queries[0, 0]
    key_rows = keys[0, 0]
    value_rows = values[0, 0]
    grad_rows = grad_out[0, 0]
    token_positions = positions[0, 0]
    length, columns = query_rows.shape
    sections = lax.axis_size("section")
    parts = lax.axis_size("mp")
    replicas = lax.axis_size("dp")
    part = lax.axis_index("mp")
    rows = length // parts
    halves = 2
    block = length // halves

    local = jnp.arange(block, dtype=jnp.int32)
    pos = token_positions.reshape(halves, block)
    allowed = (local[None, None, :] <= local[None, :, None]) & (
        local[None, None, :] >= (local[None, :] - pos)[:, :, None]
    )

    def pairs(shift):
        return [
            ((s + 1) * parts + m, s * parts + (m + shift) % parts)
            for s in range(sections - 1)
            for m in range(parts)
        ]

    width = CHUNK_HEADS * HEAD_DIM
    chunk_count = columns // width
    arrived = [[None] * chunk_count for _ in range(parts)]
    sums = []
    for c in range(chunk_count):
        cols = slice(c * width, (c + 1) * width)
        grads = chunk_grads(
            query_rows[:, cols], key_rows[:, cols], value_rows[:, cols], grad_rows[:, cols], allowed, halves
        )
        sums.append(jnp.sum(grads.astype(jnp.float32), axis=1))
        for shift in range(parts):
            target = (part + shift) % parts
            piece = lax.dynamic_slice_in_dim(grads, target * rows, rows, 1)
            arrived[shift][c] = lax.ppermute(piece, ("section", "mp"), pairs(shift))

    own = jnp.concatenate(sums, axis=1)
    slots = lax.dynamic_update_slice_in_dim(
        jnp.zeros((3, columns * parts), jnp.float32), own, part * columns, 1
    )
    totals = lax.psum(slots, ("dp", "mp"))
    totals = lax.ppermute(totals, "section", [(s + 1, s) for s in range(sections - 1)])
    bias_grad = totals / math.sqrt(replicas * length)

    received = jnp.zeros((3, rows, columns * parts), jnp.bfloat16)
    for shift in range(parts):
        source = (part - shift) % parts
        piece = jnp.concatenate(arrived[shift], axis=2)
        received = lax.dynamic_update_slice_in_dim(received, piece, source * columns, 2)
    return (received[None, None], bias_grad[None])


def solution(mesh):
    return jax.shard_map(
        per_device,
        mesh=mesh,
        in_specs=(
            P("section", "dp", None, "mp"),
            P("section", "dp", None, "mp"),
            P("section", "dp", None, "mp"),
            P("section", "dp", None, "mp"),
            P("section", "dp", None),
        ),
        out_specs=(P("section", "dp", None, "mp", None), P("section", None, None)),
        check_vma=False,
    )
```

```python
import functools
import math

import jax
import jax.numpy as jnp
from jax import lax
from jax.experimental import pallas as pl
from jax.experimental.pallas import tpu as pltpu
from jax.sharding import PartitionSpec as P

HEAD_DIM = 128
CHUNK_HEADS = 2
NT = (((1,), (1,)), ((), ()))


def grads_kernel(part_ref, pos_ref, q_ref, k_ref, v_ref, g_ref, out_ref, sum_ref, full_ref, *, parts):
    length = q_ref.shape[0]
    half = length // 2
    window = -(-half // 128) * 128
    rows = length // parts
    scaling = 1.0 / math.sqrt(HEAD_DIM)
    for b, lo in enumerate((0, length - window)):
        q = q_ref[lo : lo + window, :]
        k = k_ref[lo : lo + window, :]
        v = v_ref[lo : lo + window, :]
        g = g_ref[lo : lo + window, :]
        scores = lax.dot_general(q, k, NT, preferred_element_type=jnp.float32) * scaling
        qi = lo + lax.broadcasted_iota(jnp.int32, (window, window), 0)
        kj = lo + lax.broadcasted_iota(jnp.int32, (window, window), 1)
        start = qi - pos_ref[lo : lo + window, :]
        allowed = (kj <= qi) & (kj >= start)
        scores = jnp.where(allowed, scores, jnp.float32(-1e30))
        highest = jnp.max(scores, axis=1, keepdims=True)
        expont = jnp.exp(scores - highest)
        attn = expont / jnp.sum(expont, axis=1, keepdims=True)
        grad_v = jnp.dot(attn.T.astype(jnp.bfloat16), g, preferred_element_type=jnp.float32)
        grad_attn = lax.dot_general(g, v, NT, preferred_element_type=jnp.float32)
        delta = jnp.sum(attn * grad_attn, axis=1, keepdims=True)
        grad_scores = attn * (grad_attn - delta) * scaling
        grad_q = jnp.dot(grad_scores.astype(jnp.bfloat16), k, preferred_element_type=jnp.float32)
        grad_k = jnp.dot(grad_scores.T.astype(jnp.bfloat16), q, preferred_element_type=jnp.float32)
        keep = b * half - lo
        for i, grad in enumerate((grad_q, grad_k, grad_v)):
            full_ref[i, b * half : (b + 1) * half, :] = grad[keep : keep + half].astype(jnp.bfloat16)
    sum_ref[...] = jnp.sum(full_ref[...].astype(jnp.float32), axis=1)
    part = part_ref[0]
    for shift in range(parts):
        target = (part + shift) % parts
        out_ref[shift] = full_ref[:, pl.ds(pl.multiple_of(target * rows, 16), rows), :]


def chunk_grads(part, positions, query_rows, key_rows, value_rows, grad_rows, chunk, heads, parts):
    length = query_rows.shape[0]
    rows = length // parts
    width = heads * HEAD_DIM

    def column(h, part_ref):
        return (0, chunk * heads + h)

    in_block = pl.BlockSpec((length, HEAD_DIM), column)
    grid_spec = pltpu.PrefetchScalarGridSpec(
        num_scalar_prefetch=1,
        grid=(heads,),
        in_specs=[pl.BlockSpec((length, 1), lambda h, part_ref: (0, 0))] + [in_block] * 4,
        out_specs=[
            pl.BlockSpec((parts, 3, rows, HEAD_DIM), lambda h, part_ref: (0, 0, 0, h)),
            pl.BlockSpec((3, HEAD_DIM), lambda h, part_ref: (0, h)),
        ],
        scratch_shapes=[pltpu.VMEM((3, length, HEAD_DIM), jnp.bfloat16)],
    )
    return pl.pallas_call(
        functools.partial(grads_kernel, parts=parts),
        grid_spec=grid_spec,
        out_shape=[
            jax.ShapeDtypeStruct((parts, 3, rows, width), jnp.bfloat16),
            jax.ShapeDtypeStruct((3, width), jnp.float32),
        ],
    )(part, positions, query_rows, key_rows, value_rows, grad_rows)


def butterfly_sum(value, axis):
    count = lax.axis_size(axis)
    step = 1
    while step < count:
        value = value + lax.ppermute(value, axis, [(i, i ^ step) for i in range(count)])
        step *= 2
    return value


def per_device(queries, keys, values, grad_out, positions):
    query_rows = queries[0, 0]
    key_rows = keys[0, 0]
    value_rows = values[0, 0]
    grad_rows = grad_out[0, 0]
    token_positions = positions[0, 0].reshape(-1, 1)
    length, columns = query_rows.shape
    sections = lax.axis_size("section")
    parts = lax.axis_size("mp")
    replicas = lax.axis_size("dp")
    part = lax.axis_index("mp")
    rows = length // parts
    heads = min(CHUNK_HEADS, columns // HEAD_DIM)
    width = heads * HEAD_DIM
    chunk_count = columns // width
    part_arg = jnp.reshape(part, (1,)).astype(jnp.int32)

    def pairs(shift):
        return [
            ((s + 1) * parts + m, s * parts + (m + shift) % parts)
            for s in range(sections - 1)
            for m in range(parts)
        ]

    arrived = [[None] * chunk_count for _ in range(parts)]
    sums = []
    for c in range(chunk_count):
        grads, chunk_sums = chunk_grads(
            part_arg, token_positions, query_rows, key_rows, value_rows, grad_rows, c, heads, parts
        )
        sums.append(chunk_sums)
        for shift in range(parts):
            arrived[shift][c] = lax.ppermute(grads[shift], ("section", "mp"), pairs(shift))

    own = jnp.concatenate(sums, axis=1)
    slots = lax.dynamic_update_slice_in_dim(
        jnp.zeros((3, columns * parts), jnp.float32), own, part * columns, 1
    )
    totals = butterfly_sum(butterfly_sum(slots, "mp"), "dp")
    totals = lax.ppermute(totals, "section", [(s + 1, s) for s in range(sections - 1)])
    bias_grad = totals / math.sqrt(replicas * length)

    received = jnp.zeros((3, rows, columns * parts), jnp.bfloat16)
    for shift in range(parts):
        source = (part - shift) % parts
        for c in range(chunk_count):
            received = lax.dynamic_update_slice_in_dim(
                received, arrived[shift][c], source * columns + c * width, 2
            )
    return (received[None, None], bias_grad[None])


def solution(mesh):
    return jax.shard_map(
        per_device,
        mesh=mesh,
        in_specs=(
            P("section", "dp", None, "mp"),
            P("section", "dp", None, "mp"),
            P("section", "dp", None, "mp"),
            P("section", "dp", None, "mp"),
            P("section", "dp", None),
        ),
        out_specs=(P("section", "dp", None, "mp", None), P("section", None, None)),
        check_vma=False,
    )
```

```python
import functools
import math

import jax
import jax.numpy as jnp
from jax import lax
from jax.experimental import pallas as pl
from jax.experimental.pallas import tpu as pltpu
from jax.sharding import PartitionSpec as P

HEAD_DIM = 128
CHUNK_HEADS = 2
DEPTH = 2
NT = (((1,), (1,)), ((), ()))


def grads_kernel(part_ref, pos_ref, q_ref, k_ref, v_ref, g_ref, *refs, parts):
    out_refs, sum_ref, full_ref = refs[:parts], refs[parts], refs[parts + 1]
    length = q_ref.shape[0]
    half = length // 2
    window = -(-half // 128) * 128
    rows = length // parts
    scaling = 1.0 / math.sqrt(HEAD_DIM)
    for b, lo in enumerate((0, length - window)):
        q = q_ref[lo : lo + window, :]
        k = k_ref[lo : lo + window, :]
        v = v_ref[lo : lo + window, :]
        g = g_ref[lo : lo + window, :]
        scores = lax.dot_general(q, k, NT, preferred_element_type=jnp.float32) * scaling
        qi = lo + lax.broadcasted_iota(jnp.int32, (window, window), 0)
        kj = lo + lax.broadcasted_iota(jnp.int32, (window, window), 1)
        start = qi - pos_ref[lo : lo + window, :]
        allowed = (kj <= qi) & (kj >= start)
        scores = jnp.where(allowed, scores, jnp.float32(-1e30))
        highest = jnp.max(scores, axis=1, keepdims=True)
        expont = jnp.exp(scores - highest)
        attn = expont / jnp.sum(expont, axis=1, keepdims=True)
        grad_v = jnp.dot(attn.T.astype(jnp.bfloat16), g, preferred_element_type=jnp.float32)
        grad_attn = lax.dot_general(g, v, NT, preferred_element_type=jnp.float32)
        delta = jnp.sum(attn * grad_attn, axis=1, keepdims=True)
        grad_scores = attn * (grad_attn - delta) * scaling
        grad_q = jnp.dot(grad_scores.astype(jnp.bfloat16), k, preferred_element_type=jnp.float32)
        grad_k = jnp.dot(grad_scores.T.astype(jnp.bfloat16), q, preferred_element_type=jnp.float32)
        keep = b * half - lo
        for i, grad in enumerate((grad_q, grad_k, grad_v)):
            full_ref[i, b * half : (b + 1) * half, :] = grad[keep : keep + half].astype(jnp.bfloat16)
    sum_ref[...] = jnp.sum(full_ref[...].astype(jnp.float32), axis=1)
    part = part_ref[0]
    for shift, out_ref in enumerate(out_refs):
        target = (part + shift) % parts
        out_ref[...] = full_ref[:, pl.ds(pl.multiple_of(target * rows, 16), rows), :]


def chunk_grads(part, positions, query_rows, key_rows, value_rows, grad_rows, first, heads, parts):
    length = query_rows.shape[0]
    rows = length // parts
    width = heads * HEAD_DIM

    def column(h, part_ref):
        return (0, first + h)

    in_block = pl.BlockSpec((length, HEAD_DIM), column)
    grid_spec = pltpu.PrefetchScalarGridSpec(
        num_scalar_prefetch=1,
        grid=(heads,),
        in_specs=[pl.BlockSpec((length, 1), lambda h, part_ref: (0, 0))] + [in_block] * 4,
        out_specs=[pl.BlockSpec((3, rows, HEAD_DIM), lambda h, part_ref: (0, 0, h))] * parts
        + [pl.BlockSpec((3, HEAD_DIM), lambda h, part_ref: (0, h))],
        scratch_shapes=[pltpu.VMEM((3, length, HEAD_DIM), jnp.bfloat16)],
    )
    return pl.pallas_call(
        functools.partial(grads_kernel, parts=parts),
        grid_spec=grid_spec,
        out_shape=[jax.ShapeDtypeStruct((3, rows, width), jnp.bfloat16)] * parts
        + [jax.ShapeDtypeStruct((3, width), jnp.float32)],
    )(part, positions, query_rows, key_rows, value_rows, grad_rows)


def butterfly_sum(value, axis):
    count = lax.axis_size(axis)
    step = 1
    while step < count:
        value = value + lax.ppermute(value, axis, [(i, i ^ step) for i in range(count)])
        step *= 2
    return value


def per_device(queries, keys, values, grad_out, positions):
    query_rows = queries[0, 0]
    key_rows = keys[0, 0]
    value_rows = values[0, 0]
    grad_rows = grad_out[0, 0]
    token_positions = positions[0, 0].reshape(-1, 1)
    length, columns = query_rows.shape
    sections = lax.axis_size("section")
    parts = lax.axis_size("mp")
    replicas = lax.axis_size("dp")
    part = lax.axis_index("mp")
    rows = length // parts
    head_count = columns // HEAD_DIM
    sizes = [1] if head_count > 1 else []
    while sum(sizes) + 1 < head_count:
        sizes.append(min(CHUNK_HEADS, head_count - 1 - sum(sizes)))
    sizes.append(head_count - sum(sizes))
    firsts = [sum(sizes[:c]) for c in range(len(sizes))]
    chunk_count = len(sizes)
    part_arg = jnp.reshape(part, (1,)).astype(jnp.int32)

    def pairs(shift):
        return [
            ((s + 1) * parts + m, s * parts + (m + shift) % parts)
            for s in range(sections - 1)
            for m in range(parts)
        ]

    arrived = [[None] * chunk_count for _ in range(parts)]
    sums = []
    operands = (query_rows, key_rows, value_rows, grad_rows)
    for c in range(chunk_count):
        if c >= DEPTH:
            tied = lax.optimization_barrier((operands, [arrived[shift][c - DEPTH] for shift in range(parts)]))
            operands = tied[0]
        *grads, chunk_sums = chunk_grads(part_arg, token_positions, *operands, firsts[c], sizes[c], parts)
        sums.append(chunk_sums)
        for shift in range(parts):
            arrived[shift][c] = lax.ppermute(grads[shift], ("section", "mp"), pairs(shift))

    own = jnp.concatenate(sums, axis=1)
    slots = lax.dynamic_update_slice_in_dim(
        jnp.zeros((3, columns * parts), jnp.float32), own, part * columns, 1
    )
    totals = butterfly_sum(butterfly_sum(slots, "mp"), "dp")
    totals = lax.ppermute(totals, "section", [(s + 1, s) for s in range(sections - 1)])
    bias_grad = totals / math.sqrt(replicas * length)

    received = jnp.zeros((3, rows, columns * parts), jnp.bfloat16)
    for shift in range(parts):
        source = (part - shift) % parts
        for c in range(chunk_count):
            received = lax.dynamic_update_slice_in_dim(
                received, arrived[shift][c], source * columns + firsts[c] * HEAD_DIM, 2
            )
    return (received[None, None], bias_grad[None])


def solution(mesh):
    return jax.shard_map(
        per_device,
        mesh=mesh,
        in_specs=(
            P("section", "dp", None, "mp"),
            P("section", "dp", None, "mp"),
            P("section", "dp", None, "mp"),
            P("section", "dp", None, "mp"),
            P("section", "dp", None),
        ),
        out_specs=(P("section", "dp", None, "mp", None), P("section", None, None)),
        check_vma=False,
    )
```

```python
import functools
import math

import jax
import jax.numpy as jnp
from jax import lax
from jax.experimental import pallas as pl
from jax.experimental.pallas import tpu as pltpu
from jax.sharding import PartitionSpec as P

HEAD_DIM = 128
DEPTH = 2
NT = (((1,), (1,)), ((), ()))


def grads_kernel(part_ref, pos_ref, q_ref, k_ref, v_ref, g_ref, *refs, parts):
    out_refs, sum_ref, full_ref = refs[:parts], refs[parts], refs[parts + 1]
    length = q_ref.shape[0]
    half = length // 2
    window = -(-half // 128) * 128
    rows = length // parts
    scaling = 1.0 / math.sqrt(HEAD_DIM)
    for b, lo in enumerate((0, length - window)):
        q = q_ref[lo : lo + window, :]
        k = k_ref[lo : lo + window, :]
        v = v_ref[lo : lo + window, :]
        g = g_ref[lo : lo + window, :]
        scores = lax.dot_general(q, k, NT, preferred_element_type=jnp.float32) * scaling
        qi = lo + lax.broadcasted_iota(jnp.int32, (window, window), 0)
        kj = lo + lax.broadcasted_iota(jnp.int32, (window, window), 1)
        start = qi - pos_ref[lo : lo + window, :]
        allowed = (kj <= qi) & (kj >= start)
        scores = jnp.where(allowed, scores, jnp.float32(-1e30))
        highest = jnp.max(scores, axis=1, keepdims=True)
        expont = jnp.exp(scores - highest)
        attn = expont / jnp.sum(expont, axis=1, keepdims=True)
        grad_v = jnp.dot(attn.T.astype(jnp.bfloat16), g, preferred_element_type=jnp.float32)
        grad_attn = lax.dot_general(g, v, NT, preferred_element_type=jnp.float32)
        delta = jnp.sum(attn * grad_attn, axis=1, keepdims=True)
        grad_scores = attn * (grad_attn - delta) * scaling
        grad_q = jnp.dot(grad_scores.astype(jnp.bfloat16), k, preferred_element_type=jnp.float32)
        grad_k = jnp.dot(grad_scores.T.astype(jnp.bfloat16), q, preferred_element_type=jnp.float32)
        keep = b * half - lo
        for i, grad in enumerate((grad_q, grad_k, grad_v)):
            full_ref[i, b * half : (b + 1) * half, :] = grad[keep : keep + half].astype(jnp.bfloat16)
    sum_ref[...] = jnp.sum(full_ref[...].astype(jnp.float32), axis=1)
    part = part_ref[0]
    for shift, out_ref in enumerate(out_refs):
        target = (part + shift) % parts
        out_ref[...] = full_ref[:, pl.ds(pl.multiple_of(target * rows, 16), rows), :]


def chunk_grads(part, positions, query_rows, key_rows, value_rows, grad_rows, first, heads, parts):
    length = query_rows.shape[0]
    rows = length // parts
    width = heads * HEAD_DIM

    def column(h, part_ref):
        return (0, first + h)

    in_block = pl.BlockSpec((length, HEAD_DIM), column)
    grid_spec = pltpu.PrefetchScalarGridSpec(
        num_scalar_prefetch=1,
        grid=(heads,),
        in_specs=[pl.BlockSpec((length, 1), lambda h, part_ref: (0, 0))] + [in_block] * 4,
        out_specs=[pl.BlockSpec((3, rows, HEAD_DIM), lambda h, part_ref: (0, 0, h))] * parts
        + [pl.BlockSpec((3, HEAD_DIM), lambda h, part_ref: (0, h))],
        scratch_shapes=[pltpu.VMEM((3, length, HEAD_DIM), jnp.bfloat16)],
    )
    return pl.pallas_call(
        functools.partial(grads_kernel, parts=parts),
        grid_spec=grid_spec,
        out_shape=[jax.ShapeDtypeStruct((3, rows, width), jnp.bfloat16)] * parts
        + [jax.ShapeDtypeStruct((3, width), jnp.float32)],
    )(part, positions, query_rows, key_rows, value_rows, grad_rows)


def butterfly_sum(value, axis):
    count = lax.axis_size(axis)
    step = 1
    while step < count:
        value = value + lax.ppermute(value, axis, [(i, i ^ step) for i in range(count)])
        step *= 2
    return value


def per_device(queries, keys, values, grad_out, positions):
    query_rows = queries[0, 0]
    key_rows = keys[0, 0]
    value_rows = values[0, 0]
    grad_rows = grad_out[0, 0]
    token_positions = positions[0, 0].reshape(-1, 1)
    length, columns = query_rows.shape
    sections = lax.axis_size("section")
    parts = lax.axis_size("mp")
    replicas = lax.axis_size("dp")
    part = lax.axis_index("mp")
    rows = length // parts
    head_count = columns // HEAD_DIM
    sizes = [1]
    while sum(sizes) < head_count:
        sizes.append(min(2 * sizes[-1] + 1, head_count - sum(sizes)))
    firsts = [sum(sizes[:c]) for c in range(len(sizes))]
    chunk_count = len(sizes)
    part_arg = jnp.reshape(part, (1,)).astype(jnp.int32)

    def pairs(shift):
        return [
            ((s + 1) * parts + m, s * parts + (m + shift) % parts)
            for s in range(sections - 1)
            for m in range(parts)
        ]

    arrived = [[None] * chunk_count for _ in range(parts)]
    sums = []
    operands = (query_rows, key_rows, value_rows, grad_rows)
    for c in range(chunk_count):
        if c >= DEPTH:
            tied = lax.optimization_barrier((operands, [arrived[shift][c - DEPTH] for shift in range(parts)]))
            operands = tied[0]
        *grads, chunk_sums = chunk_grads(part_arg, token_positions, *operands, firsts[c], sizes[c], parts)
        sums.append(chunk_sums)
        for shift in range(parts):
            arrived[shift][c] = lax.ppermute(grads[shift], ("section", "mp"), pairs(shift))

    own = jnp.concatenate(sums, axis=1)
    if chunk_count > 1:
        own = lax.optimization_barrier((own, [arrived[shift][-2] for shift in range(parts)]))[0]
    own = butterfly_sum(own, "dp")
    totals = jnp.zeros((3, columns * parts), jnp.float32)
    for shift in range(parts):
        source = (part - shift) % parts
        piece = lax.ppermute(own, ("section", "mp"), pairs(shift))
        totals = lax.dynamic_update_slice_in_dim(totals, piece, source * columns, 1)
    bias_grad = totals / math.sqrt(replicas * length)

    received = jnp.zeros((3, rows, columns * parts), jnp.bfloat16)
    for shift in range(parts):
        source = (part - shift) % parts
        for c in range(chunk_count):
            received = lax.dynamic_update_slice_in_dim(
                received, arrived[shift][c], source * columns + firsts[c] * HEAD_DIM, 2
            )
    return (received[None, None], bias_grad[None])


def solution(mesh):
    return jax.shard_map(
        per_device,
        mesh=mesh,
        in_specs=(
            P("section", "dp", None, "mp"),
            P("section", "dp", None, "mp"),
            P("section", "dp", None, "mp"),
            P("section", "dp", None, "mp"),
            P("section", "dp", None),
        ),
        out_specs=(P("section", "dp", None, "mp", None), P("section", None, None)),
        check_vma=False,
    )
```

```python
import functools
import math

import jax
import jax.numpy as jnp
from jax import lax
from jax.experimental import pallas as pl
from jax.experimental.pallas import tpu as pltpu
from jax.sharding import PartitionSpec as P

HEAD_DIM = 128
DEPTH = 2
NT = (((1,), (1,)), ((), ()))


def grads_kernel(part_ref, pos_ref, q_ref, k_ref, v_ref, g_ref, *refs, parts):
    out_refs, sum_ref, full_ref = refs[:parts], refs[parts], refs[parts + 1]
    length = q_ref.shape[0]
    half = length // 2
    window = -(-half // 128) * 128
    rows = length // parts
    scaling = 1.0 / math.sqrt(HEAD_DIM)
    for b, lo in enumerate((0, length - window)):
        q = q_ref[lo : lo + window, :]
        k = k_ref[lo : lo + window, :]
        v = v_ref[lo : lo + window, :]
        g = g_ref[lo : lo + window, :]
        scores = lax.dot_general(q, k, NT, preferred_element_type=jnp.float32) * scaling
        qi = lo + lax.broadcasted_iota(jnp.int32, (window, window), 0)
        kj = lo + lax.broadcasted_iota(jnp.int32, (window, window), 1)
        start = qi - pos_ref[lo : lo + window, :]
        allowed = (kj <= qi) & (kj >= start)
        scores = jnp.where(allowed, scores, jnp.float32(-1e30))
        highest = jnp.max(scores, axis=1, keepdims=True)
        expont = jnp.exp(scores - highest)
        attn = expont / jnp.sum(expont, axis=1, keepdims=True)
        grad_v = jnp.dot(attn.T.astype(jnp.bfloat16), g, preferred_element_type=jnp.float32)
        grad_attn = lax.dot_general(g, v, NT, preferred_element_type=jnp.float32)
        delta = jnp.sum(attn * grad_attn, axis=1, keepdims=True)
        grad_scores = attn * (grad_attn - delta) * scaling
        grad_q = jnp.dot(grad_scores.astype(jnp.bfloat16), k, preferred_element_type=jnp.float32)
        grad_k = jnp.dot(grad_scores.T.astype(jnp.bfloat16), q, preferred_element_type=jnp.float32)
        keep = b * half - lo
        for i, grad in enumerate((grad_q, grad_k, grad_v)):
            full_ref[i, b * half : (b + 1) * half, :] = grad[keep : keep + half].astype(jnp.bfloat16)
    sum_ref[...] = jnp.sum(full_ref[...].astype(jnp.float32), axis=1)
    part = part_ref[0]
    for shift, out_ref in enumerate(out_refs):
        target = (part + shift) % parts
        out_ref[...] = full_ref[:, pl.ds(pl.multiple_of(target * rows, 16), rows), :]


def chunk_grads(part, positions, query_rows, key_rows, value_rows, grad_rows, first, heads, parts):
    length = query_rows.shape[0]
    rows = length // parts
    width = heads * HEAD_DIM

    def column(h, part_ref):
        return (0, first + h)

    in_block = pl.BlockSpec((length, HEAD_DIM), column)
    grid_spec = pltpu.PrefetchScalarGridSpec(
        num_scalar_prefetch=1,
        grid=(heads,),
        in_specs=[pl.BlockSpec((length, 1), lambda h, part_ref: (0, 0))] + [in_block] * 4,
        out_specs=[pl.BlockSpec((3, rows, HEAD_DIM), lambda h, part_ref: (0, 0, h))] * parts
        + [pl.BlockSpec((3, HEAD_DIM), lambda h, part_ref: (0, h))],
        scratch_shapes=[pltpu.VMEM((3, length, HEAD_DIM), jnp.bfloat16)],
    )
    return pl.pallas_call(
        functools.partial(grads_kernel, parts=parts),
        grid_spec=grid_spec,
        out_shape=[jax.ShapeDtypeStruct((3, rows, width), jnp.bfloat16)] * parts
        + [jax.ShapeDtypeStruct((3, width), jnp.float32)],
    )(part, positions, query_rows, key_rows, value_rows, grad_rows)


def butterfly_sum(value, axis):
    count = lax.axis_size(axis)
    step = 1
    while step < count:
        value = value + lax.ppermute(value, axis, [(i, i ^ step) for i in range(count)])
        step *= 2
    return value


def per_device(queries, keys, values, grad_out, positions):
    query_rows = queries[0, 0]
    key_rows = keys[0, 0]
    value_rows = values[0, 0]
    grad_rows = grad_out[0, 0]
    token_positions = positions[0, 0].reshape(-1, 1)
    length, columns = query_rows.shape
    sections = lax.axis_size("section")
    parts = lax.axis_size("mp")
    replicas = lax.axis_size("dp")
    part = lax.axis_index("mp")
    rows = length // parts
    head_count = columns // HEAD_DIM
    sizes = [1]
    while sum(sizes) < head_count:
        sizes.append(min(2 * sizes[-1] + 1, head_count - sum(sizes)))
    firsts = [sum(sizes[:c]) for c in range(len(sizes))]
    chunk_count = len(sizes)
    part_arg = jnp.reshape(part, (1,)).astype(jnp.int32)

    def pairs(shift):
        return [
            ((s + 1) * parts + m, s * parts + (m + shift) % parts)
            for s in range(sections - 1)
            for m in range(parts)
        ]

    arrived = [[None] * chunk_count for _ in range(parts)]
    sums = []
    operands = (query_rows, key_rows, value_rows, grad_rows)
    for c in range(chunk_count):
        if c >= DEPTH:
            tied = lax.optimization_barrier((operands, [arrived[shift][c - DEPTH] for shift in range(parts)]))
            operands = tied[0]
        *grads, chunk_sums = chunk_grads(part_arg, token_positions, *operands, firsts[c], sizes[c], parts)
        sums.append(chunk_sums)
        for shift in range(parts):
            arrived[shift][c] = lax.ppermute(grads[shift], ("section", "mp"), pairs(shift))

    own = jnp.concatenate(sums, axis=1)
    section = lax.axis_index("section")
    slots = jnp.zeros((sections, 3, columns * parts), jnp.float32)
    slots = lax.dynamic_update_slice(slots, own[None], (section - 1, 0, part * columns))
    slots = jnp.where(section > 0, slots, 0.0)
    totals = lax.psum(slots, ("section", "dp", "mp"))
    totals = lax.dynamic_index_in_dim(totals, section, 0, keepdims=False)
    bias_grad = totals / math.sqrt(replicas * length)

    received = jnp.zeros((3, rows, columns * parts), jnp.bfloat16)
    for shift in range(parts):
        source = (part - shift) % parts
        for c in range(chunk_count):
            received = lax.dynamic_update_slice_in_dim(
                received, arrived[shift][c], source * columns + firsts[c] * HEAD_DIM, 2
            )
    return (received[None, None], bias_grad[None])


def solution(mesh):
    return jax.shard_map(
        per_device,
        mesh=mesh,
        in_specs=(
            P("section", "dp", None, "mp"),
            P("section", "dp", None, "mp"),
            P("section", "dp", None, "mp"),
            P("section", "dp", None, "mp"),
            P("section", "dp", None),
        ),
        out_specs=(P("section", "dp", None, "mp", None), P("section", None, None)),
        check_vma=False,
    )
```

```python
import functools
import math

import jax
import jax.numpy as jnp
from jax import lax
from jax.experimental import pallas as pl
from jax.experimental.pallas import tpu as pltpu
from jax.sharding import PartitionSpec as P

HEAD_DIM = 128
NT = (((1,), (1,)), ((), ()))


def grads_kernel(part_ref, pos_ref, q_ref, k_ref, v_ref, g_ref, *refs, parts):
    out_refs, sum_ref, full_ref = refs[:parts], refs[parts], refs[parts + 1]
    length = q_ref.shape[0]
    half = length // 2
    window = -(-half // 128) * 128
    rows = length // parts
    scaling = 1.0 / math.sqrt(HEAD_DIM)
    for b, lo in enumerate((0, length - window)):
        q = q_ref[lo : lo + window, :]
        k = k_ref[lo : lo + window, :]
        v = v_ref[lo : lo + window, :]
        g = g_ref[lo : lo + window, :]
        scores = lax.dot_general(q, k, NT, preferred_element_type=jnp.float32) * scaling
        qi = lo + lax.broadcasted_iota(jnp.int32, (window, window), 0)
        kj = lo + lax.broadcasted_iota(jnp.int32, (window, window), 1)
        start = qi - pos_ref[lo : lo + window, :]
        allowed = (kj <= qi) & (kj >= start)
        scores = jnp.where(allowed, scores, jnp.float32(-1e30))
        highest = jnp.max(scores, axis=1, keepdims=True)
        expont = jnp.exp(scores - highest)
        attn = expont / jnp.sum(expont, axis=1, keepdims=True)
        grad_v = jnp.dot(attn.T.astype(jnp.bfloat16), g, preferred_element_type=jnp.float32)
        grad_attn = lax.dot_general(g, v, NT, preferred_element_type=jnp.float32)
        delta = jnp.sum(attn * grad_attn, axis=1, keepdims=True)
        grad_scores = attn * (grad_attn - delta) * scaling
        grad_q = jnp.dot(grad_scores.astype(jnp.bfloat16), k, preferred_element_type=jnp.float32)
        grad_k = jnp.dot(grad_scores.T.astype(jnp.bfloat16), q, preferred_element_type=jnp.float32)
        keep = b * half - lo
        for i, grad in enumerate((grad_q, grad_k, grad_v)):
            full_ref[i, b * half : (b + 1) * half, :] = grad[keep : keep + half].astype(jnp.bfloat16)
    sum_ref[...] = jnp.sum(full_ref[...].astype(jnp.float32), axis=1)
    part = part_ref[0]
    for shift, out_ref in enumerate(out_refs):
        target = (part + shift) % parts
        out_ref[...] = full_ref[:, pl.ds(pl.multiple_of(target * rows, 16), rows), :]


def chunk_grads(part, positions, query_rows, key_rows, value_rows, grad_rows, first, heads, parts):
    length = query_rows.shape[0]
    rows = length // parts
    width = heads * HEAD_DIM

    def column(h, part_ref):
        return (0, first + h)

    in_block = pl.BlockSpec((length, HEAD_DIM), column)
    grid_spec = pltpu.PrefetchScalarGridSpec(
        num_scalar_prefetch=1,
        grid=(heads,),
        in_specs=[pl.BlockSpec((length, 1), lambda h, part_ref: (0, 0))] + [in_block] * 4,
        out_specs=[pl.BlockSpec((3, rows, HEAD_DIM), lambda h, part_ref: (0, 0, h))] * parts
        + [pl.BlockSpec((3, HEAD_DIM), lambda h, part_ref: (0, h))],
        scratch_shapes=[pltpu.VMEM((3, length, HEAD_DIM), jnp.bfloat16)],
    )
    return pl.pallas_call(
        functools.partial(grads_kernel, parts=parts),
        grid_spec=grid_spec,
        out_shape=[jax.ShapeDtypeStruct((3, rows, width), jnp.bfloat16)] * parts
        + [jax.ShapeDtypeStruct((3, width), jnp.float32)],
    )(part, positions, query_rows, key_rows, value_rows, grad_rows)


def per_device(queries, keys, values, grad_out, positions):
    query_rows = queries[0, 0]
    key_rows = keys[0, 0]
    value_rows = values[0, 0]
    grad_rows = grad_out[0, 0]
    token_positions = positions[0, 0].reshape(-1, 1)
    length, columns = query_rows.shape
    sections = lax.axis_size("section")
    parts = lax.axis_size("mp")
    replicas = lax.axis_size("dp")
    part = lax.axis_index("mp")
    rows = length // parts
    head_count = columns // HEAD_DIM
    lead = max(1, head_count // 4)
    sizes = [lead, head_count - lead] if head_count > lead else [head_count]
    firsts = [sum(sizes[:c]) for c in range(len(sizes))]
    chunk_count = len(sizes)
    part_arg = jnp.reshape(part, (1,)).astype(jnp.int32)

    def pairs(shift):
        return [
            ((s + 1) * parts + m, s * parts + (m + shift) % parts)
            for s in range(sections - 1)
            for m in range(parts)
        ]

    arrived = [[None] * chunk_count for _ in range(parts)]
    sums = []
    for c in range(chunk_count):
        *grads, chunk_sums = chunk_grads(
            part_arg, token_positions, query_rows, key_rows, value_rows, grad_rows, firsts[c], sizes[c], parts
        )
        sums.append(chunk_sums)
        tie = []
        if c == chunk_count - 1:
            own = jnp.concatenate(sums, axis=1)
            if c > 0:
                own = lax.optimization_barrier((own, [arrived[shift][c - 1] for shift in range(parts)]))[0]
            relayed = lax.ppermute(own, "section", [(s + 1, s) for s in range(sections - 1)])
            tie.append(relayed)
        if c > 0:
            tie += [arrived[shift][c - 1] for shift in range(parts)]
        if tie:
            grads = lax.optimization_barrier((grads, tie))[0]
        for shift in range(parts):
            arrived[shift][c] = lax.ppermute(grads[shift], ("section", "mp"), pairs(shift))

    def receivers_sum(value, axis):
        count = lax.axis_size(axis)
        step = 1
        while step < count:
            ring = [(s * count + i, s * count + (i ^ step)) for s in range(sections - 1) for i in range(count)]
            value = value + lax.ppermute(value, ("section", axis), ring)
            step *= 2
        return value

    if chunk_count > 1:
        relayed = lax.optimization_barrier((relayed, arrived[0][-1]))[0]
    reduced = receivers_sum(relayed, "dp")
    slots = lax.dynamic_update_slice_in_dim(
        jnp.zeros((3, columns * parts), jnp.float32), reduced, part * columns, 1
    )
    totals = receivers_sum(slots, "mp")
    bias_grad = totals / math.sqrt(replicas * length)

    received = jnp.zeros((3, rows, columns * parts), jnp.bfloat16)
    for shift in range(parts):
        source = (part - shift) % parts
        for c in range(chunk_count):
            received = lax.dynamic_update_slice_in_dim(
                received, arrived[shift][c], source * columns + firsts[c] * HEAD_DIM, 2
            )
    return (received[None, None], bias_grad[None])


def solution(mesh):
    return jax.shard_map(
        per_device,
        mesh=mesh,
        in_specs=(
            P("section", "dp", None, "mp"),
            P("section", "dp", None, "mp"),
            P("section", "dp", None, "mp"),
            P("section", "dp", None, "mp"),
            P("section", "dp", None),
        ),
        out_specs=(P("section", "dp", None, "mp", None), P("section", None, None)),
        check_vma=False,
    )
```

```python
import functools
import math

import jax
import jax.numpy as jnp
from jax import lax
from jax.experimental import pallas as pl
from jax.experimental.pallas import tpu as pltpu
from jax.sharding import PartitionSpec as P

HEAD_DIM = 128
NT = (((1,), (1,)), ((), ()))


def grads_kernel(part_ref, pos_ref, q_ref, k_ref, v_ref, g_ref, *refs, parts):
    out_refs, sum_ref, full_ref = refs[:parts], refs[parts], refs[parts + 1]
    length = q_ref.shape[0]
    half = length // 2
    window = -(-half // 128) * 128
    rows = length // parts
    scaling = 1.0 / math.sqrt(HEAD_DIM)
    for b, lo in enumerate((0, length - window)):
        q = q_ref[lo : lo + window, :]
        k = k_ref[lo : lo + window, :]
        v = v_ref[lo : lo + window, :]
        g = g_ref[lo : lo + window, :]
        scores = lax.dot_general(q, k, NT, preferred_element_type=jnp.float32) * scaling
        qi = lo + lax.broadcasted_iota(jnp.int32, (window, window), 0)
        kj = lo + lax.broadcasted_iota(jnp.int32, (window, window), 1)
        start = qi - pos_ref[lo : lo + window, :]
        allowed = (kj <= qi) & (kj >= start)
        scores = jnp.where(allowed, scores, jnp.float32(-1e30))
        highest = jnp.max(scores, axis=1, keepdims=True)
        expont = jnp.exp(scores - highest)
        attn = expont / jnp.sum(expont, axis=1, keepdims=True)
        grad_v = jnp.dot(attn.T.astype(jnp.bfloat16), g, preferred_element_type=jnp.float32)
        grad_attn = lax.dot_general(g, v, NT, preferred_element_type=jnp.float32)
        delta = jnp.sum(attn * grad_attn, axis=1, keepdims=True)
        grad_scores = attn * (grad_attn - delta) * scaling
        grad_q = jnp.dot(grad_scores.astype(jnp.bfloat16), k, preferred_element_type=jnp.float32)
        grad_k = jnp.dot(grad_scores.T.astype(jnp.bfloat16), q, preferred_element_type=jnp.float32)
        keep = b * half - lo
        for i, grad in enumerate((grad_q, grad_k, grad_v)):
            full_ref[i, b * half : (b + 1) * half, :] = grad[keep : keep + half].astype(jnp.bfloat16)
    sum_ref[...] = jnp.sum(full_ref[...].astype(jnp.float32), axis=1)
    part = part_ref[0]
    for shift, out_ref in enumerate(out_refs):
        target = (part + shift) % parts
        out_ref[...] = full_ref[:, pl.ds(pl.multiple_of(target * rows, 16), rows), :]


def chunk_grads(part, positions, query_rows, key_rows, value_rows, grad_rows, first, heads, parts):
    length = query_rows.shape[0]
    rows = length // parts
    width = heads * HEAD_DIM

    def column(h, part_ref):
        return (0, first + h)

    in_block = pl.BlockSpec((length, HEAD_DIM), column)
    grid_spec = pltpu.PrefetchScalarGridSpec(
        num_scalar_prefetch=1,
        grid=(heads,),
        in_specs=[pl.BlockSpec((length, 1), lambda h, part_ref: (0, 0))] + [in_block] * 4,
        out_specs=[pl.BlockSpec((3, rows, HEAD_DIM), lambda h, part_ref: (0, 0, h))] * parts
        + [pl.BlockSpec((3, HEAD_DIM), lambda h, part_ref: (0, h))],
        scratch_shapes=[pltpu.VMEM((3, length, HEAD_DIM), jnp.bfloat16)],
    )
    return pl.pallas_call(
        functools.partial(grads_kernel, parts=parts),
        grid_spec=grid_spec,
        out_shape=[jax.ShapeDtypeStruct((3, rows, width), jnp.bfloat16)] * parts
        + [jax.ShapeDtypeStruct((3, width), jnp.float32)],
    )(part, positions, query_rows, key_rows, value_rows, grad_rows)


def per_device(queries, keys, values, grad_out, positions):
    query_rows = queries[0, 0]
    key_rows = keys[0, 0]
    value_rows = values[0, 0]
    grad_rows = grad_out[0, 0]
    token_positions = positions[0, 0].reshape(-1, 1)
    length, columns = query_rows.shape
    sections = lax.axis_size("section")
    parts = lax.axis_size("mp")
    replicas = lax.axis_size("dp")
    part = lax.axis_index("mp")
    rows = length // parts
    head_count = columns // HEAD_DIM
    lead = max(1, head_count // 4)
    sizes = [lead, head_count - lead] if head_count > lead else [head_count]
    firsts = [sum(sizes[:c]) for c in range(len(sizes))]
    chunk_count = len(sizes)
    part_arg = jnp.reshape(part, (1,)).astype(jnp.int32)

    def pairs(shift):
        return [
            ((s + 1) * parts + m, s * parts + (m + shift) % parts)
            for s in range(sections - 1)
            for m in range(parts)
        ]

    arrived = [[None] * chunk_count for _ in range(parts)]
    sums = []
    for c in range(chunk_count):
        *grads, chunk_sums = chunk_grads(
            part_arg, token_positions, query_rows, key_rows, value_rows, grad_rows, firsts[c], sizes[c], parts
        )
        sums.append(chunk_sums)
        tie = []
        if c == chunk_count - 1:
            own = jnp.concatenate(sums, axis=1)
            relayed = lax.ppermute(own, "section", [(s + 1, s) for s in range(sections - 1)])
            tie.append(relayed)
        if c > 0:
            tie += [arrived[shift][c - 1] for shift in range(parts)]
        if tie:
            grads = lax.optimization_barrier((grads, tie))[0]
        for shift in range(parts):
            arrived[shift][c] = lax.ppermute(grads[shift], ("section", "mp"), pairs(shift))

    def receivers_sum(value, axis):
        count = lax.axis_size(axis)
        step = 1
        while step < count:
            ring = [(s * count + i, s * count + (i ^ step)) for s in range(sections - 1) for i in range(count)]
            value = value + lax.ppermute(value, ("section", axis), ring)
            step *= 2
        return value

    if chunk_count > 1:
        relayed = lax.optimization_barrier((relayed, arrived[0][-1]))[0]
    reduced = receivers_sum(relayed, "dp")
    slots = lax.dynamic_update_slice_in_dim(
        jnp.zeros((3, columns * parts), jnp.float32), reduced, part * columns, 1
    )
    totals = receivers_sum(slots, "mp")
    bias_grad = totals / math.sqrt(replicas * length)

    received = jnp.zeros((3, rows, columns * parts), jnp.bfloat16)
    for shift in range(parts):
        source = (part - shift) % parts
        for c in range(chunk_count):
            received = lax.dynamic_update_slice_in_dim(
                received, arrived[shift][c], source * columns + firsts[c] * HEAD_DIM, 2
            )
    return (received[None, None], bias_grad[None])


def solution(mesh):
    return jax.shard_map(
        per_device,
        mesh=mesh,
        in_specs=(
            P("section", "dp", None, "mp"),
            P("section", "dp", None, "mp"),
            P("section", "dp", None, "mp"),
            P("section", "dp", None, "mp"),
            P("section", "dp", None),
        ),
        out_specs=(P("section", "dp", None, "mp", None), P("section", None, None)),
        check_vma=False,
    )
```

```python
import functools
import math

import jax
import jax.numpy as jnp
from jax import lax
from jax.experimental import pallas as pl
from jax.experimental.pallas import tpu as pltpu
from jax.sharding import PartitionSpec as P

HEAD_DIM = 128
NT = (((1,), (1,)), ((), ()))


def grads_kernel(part_ref, pos_ref, q_ref, k_ref, v_ref, g_ref, *refs, parts):
    out_refs, sum_ref, full_ref = refs[:parts], refs[parts], refs[parts + 1]
    length = q_ref.shape[0]
    half = length // 2
    window = -(-half // 128) * 128
    rows = length // parts
    scaling = 1.0 / math.sqrt(HEAD_DIM)
    for b, lo in enumerate((0, length - window)):
        q = q_ref[lo : lo + window, :]
        k = k_ref[lo : lo + window, :]
        v = v_ref[lo : lo + window, :]
        g = g_ref[lo : lo + window, :]
        scores = lax.dot_general(k, q, NT, preferred_element_type=jnp.float32) * scaling
        kj = lo + lax.broadcasted_iota(jnp.int32, (window, window), 0)
        qi = lo + lax.broadcasted_iota(jnp.int32, (window, window), 1)
        start = lo + lax.broadcasted_iota(jnp.int32, (1, window), 1) - pos_ref[:, lo : lo + window]
        allowed = (kj <= qi) & (kj >= start)
        scores = jnp.where(allowed, scores, jnp.float32(-1e30))
        highest = jnp.max(scores, axis=0, keepdims=True)
        expont = jnp.exp(scores - highest)
        attn = expont / jnp.sum(expont, axis=0, keepdims=True)
        grad_v = jnp.dot(attn.astype(jnp.bfloat16), g, preferred_element_type=jnp.float32)
        grad_attn = lax.dot_general(v, g, NT, preferred_element_type=jnp.float32)
        delta = jnp.sum(attn * grad_attn, axis=0, keepdims=True)
        grad_scores = attn * (grad_attn - delta) * scaling
        grad_k = jnp.dot(grad_scores.astype(jnp.bfloat16), q, preferred_element_type=jnp.float32)
        grad_q = jnp.dot(grad_scores.T.astype(jnp.bfloat16), k, preferred_element_type=jnp.float32)
        keep = b * half - lo
        for i, grad in enumerate((grad_q, grad_k, grad_v)):
            full_ref[i, b * half : (b + 1) * half, :] = grad[keep : keep + half].astype(jnp.bfloat16)
    sum_ref[...] = jnp.sum(full_ref[...].astype(jnp.float32), axis=1)
    part = part_ref[0]
    for shift, out_ref in enumerate(out_refs):
        target = (part + shift) % parts
        out_ref[...] = full_ref[:, pl.ds(pl.multiple_of(target * rows, 16), rows), :]


def chunk_grads(part, positions, query_rows, key_rows, value_rows, grad_rows, first, heads, parts):
    length = query_rows.shape[0]
    rows = length // parts
    width = heads * HEAD_DIM

    def column(h, part_ref):
        return (0, first + h)

    in_block = pl.BlockSpec((length, HEAD_DIM), column)
    grid_spec = pltpu.PrefetchScalarGridSpec(
        num_scalar_prefetch=1,
        grid=(heads,),
        in_specs=[pl.BlockSpec((1, length), lambda h, part_ref: (0, 0))] + [in_block] * 4,
        out_specs=[pl.BlockSpec((3, rows, HEAD_DIM), lambda h, part_ref: (0, 0, h))] * parts
        + [pl.BlockSpec((3, HEAD_DIM), lambda h, part_ref: (0, h))],
        scratch_shapes=[pltpu.VMEM((3, length, HEAD_DIM), jnp.bfloat16)],
    )
    return pl.pallas_call(
        functools.partial(grads_kernel, parts=parts),
        grid_spec=grid_spec,
        out_shape=[jax.ShapeDtypeStruct((3, rows, width), jnp.bfloat16)] * parts
        + [jax.ShapeDtypeStruct((3, width), jnp.float32)],
    )(part, positions, query_rows, key_rows, value_rows, grad_rows)


def per_device(queries, keys, values, grad_out, positions):
    query_rows = queries[0, 0]
    key_rows = keys[0, 0]
    value_rows = values[0, 0]
    grad_rows = grad_out[0, 0]
    token_positions = positions[0, 0].reshape(1, -1)
    length, columns = query_rows.shape
    sections = lax.axis_size("section")
    parts = lax.axis_size("mp")
    replicas = lax.axis_size("dp")
    part = lax.axis_index("mp")
    rows = length // parts
    head_count = columns // HEAD_DIM
    lead = max(1, head_count // 4)
    sizes = [lead, head_count - lead] if head_count > lead else [head_count]
    firsts = [sum(sizes[:c]) for c in range(len(sizes))]
    chunk_count = len(sizes)
    part_arg = jnp.reshape(part, (1,)).astype(jnp.int32)

    def pairs(shift):
        return [
            ((s + 1) * parts + m, s * parts + (m + shift) % parts)
            for s in range(sections - 1)
            for m in range(parts)
        ]

    arrived = [[None] * chunk_count for _ in range(parts)]
    sums = []
    for c in range(chunk_count):
        *grads, chunk_sums = chunk_grads(
            part_arg, token_positions, query_rows, key_rows, value_rows, grad_rows, firsts[c], sizes[c], parts
        )
        sums.append(chunk_sums)
        tie = []
        if c == chunk_count - 1:
            own = jnp.concatenate(sums, axis=1)
            relayed = lax.ppermute(own, "section", [(s + 1, s) for s in range(sections - 1)])
            tie.append(relayed)
        if c > 0:
            tie += [arrived[shift][c - 1] for shift in range(parts)]
        if tie:
            grads = lax.optimization_barrier((grads, tie))[0]
        for shift in range(parts):
            arrived[shift][c] = lax.ppermute(grads[shift], ("section", "mp"), pairs(shift))

    def receivers_sum(value, axis):
        count = lax.axis_size(axis)
        step = 1
        while step < count:
            ring = [(s * count + i, s * count + (i ^ step)) for s in range(sections - 1) for i in range(count)]
            value = value + lax.ppermute(value, ("section", axis), ring)
            step *= 2
        return value

    if chunk_count > 1:
        relayed = lax.optimization_barrier((relayed, arrived[0][-1]))[0]
    reduced = receivers_sum(relayed, "dp")
    slots = lax.dynamic_update_slice_in_dim(
        jnp.zeros((3, columns * parts), jnp.float32), reduced, part * columns, 1
    )
    totals = receivers_sum(slots, "mp")
    bias_grad = totals / math.sqrt(replicas * length)

    received = jnp.zeros((3, rows, columns * parts), jnp.bfloat16)
    for shift in range(parts):
        source = (part - shift) % parts
        for c in range(chunk_count):
            received = lax.dynamic_update_slice_in_dim(
                received, arrived[shift][c], source * columns + firsts[c] * HEAD_DIM, 2
            )
    return (received[None, None], bias_grad[None])


def solution(mesh):
    return jax.shard_map(
        per_device,
        mesh=mesh,
        in_specs=(
            P("section", "dp", None, "mp"),
            P("section", "dp", None, "mp"),
            P("section", "dp", None, "mp"),
            P("section", "dp", None, "mp"),
            P("section", "dp", None),
        ),
        out_specs=(P("section", "dp", None, "mp", None), P("section", None, None)),
        check_vma=False,
    )
```

```python
import functools
import math

import jax
import jax.numpy as jnp
from jax import lax
from jax.experimental import pallas as pl
from jax.experimental.pallas import tpu as pltpu
from jax.sharding import PartitionSpec as P

HEAD_DIM = 128
NT = (((1,), (1,)), ((), ()))


def grads_kernel(part_ref, pos_ref, q_ref, k_ref, v_ref, g_ref, *refs, parts):
    out_refs, sum_ref, full_ref = refs[:parts], refs[parts], refs[parts + 1]
    length = q_ref.shape[0]
    half = length // 2
    window = -(-half // 128) * 128
    rows = length // parts
    scaling = 1.0 / math.sqrt(HEAD_DIM)
    for b, lo in enumerate((0, length - window)):
        klo = b * half
        q = q_ref[lo : lo + window, :]
        g = g_ref[lo : lo + window, :]
        k = k_ref[klo : klo + half, :]
        v = v_ref[klo : klo + half, :]
        scores = lax.dot_general(k, q, NT, preferred_element_type=jnp.float32) * scaling
        kj = klo + lax.broadcasted_iota(jnp.int32, (half, window), 0)
        qi = lo + lax.broadcasted_iota(jnp.int32, (half, window), 1)
        start = lo + lax.broadcasted_iota(jnp.int32, (1, window), 1) - pos_ref[:, lo : lo + window]
        allowed = (kj <= qi) & (kj >= start)
        scores = jnp.where(allowed, scores, jnp.float32(-1e30))
        highest = jnp.max(scores, axis=0, keepdims=True)
        expont = jnp.exp(scores - highest)
        attn = expont / jnp.sum(expont, axis=0, keepdims=True)
        query = lo + lax.broadcasted_iota(jnp.int32, (1, window), 1)
        attn = jnp.where((query >= klo) & (query < klo + half), attn, jnp.float32(0.0))
        grad_v = jnp.dot(attn.astype(jnp.bfloat16), g, preferred_element_type=jnp.float32)
        grad_attn = lax.dot_general(v, g, NT, preferred_element_type=jnp.float32)
        delta = jnp.sum(attn * grad_attn, axis=0, keepdims=True)
        grad_scores = attn * (grad_attn - delta) * scaling
        grad_k = jnp.dot(grad_scores.astype(jnp.bfloat16), q, preferred_element_type=jnp.float32)
        grad_q = jnp.dot(grad_scores.T.astype(jnp.bfloat16), k, preferred_element_type=jnp.float32)
        keep = b * half - lo
        full_ref[0, b * half : (b + 1) * half, :] = grad_q[keep : keep + half].astype(jnp.bfloat16)
        full_ref[1, b * half : (b + 1) * half, :] = grad_k.astype(jnp.bfloat16)
        full_ref[2, b * half : (b + 1) * half, :] = grad_v.astype(jnp.bfloat16)
    sum_ref[...] = jnp.sum(full_ref[...].astype(jnp.float32), axis=1)
    part = part_ref[0]
    for shift, out_ref in enumerate(out_refs):
        target = (part + shift) % parts
        out_ref[...] = full_ref[:, pl.ds(pl.multiple_of(target * rows, 16), rows), :]


def chunk_grads(part, positions, query_rows, key_rows, value_rows, grad_rows, first, heads, parts):
    length = query_rows.shape[0]
    rows = length // parts
    width = heads * HEAD_DIM

    def column(h, part_ref):
        return (0, first + h)

    in_block = pl.BlockSpec((length, HEAD_DIM), column)
    grid_spec = pltpu.PrefetchScalarGridSpec(
        num_scalar_prefetch=1,
        grid=(heads,),
        in_specs=[pl.BlockSpec((1, length), lambda h, part_ref: (0, 0))] + [in_block] * 4,
        out_specs=[pl.BlockSpec((3, rows, HEAD_DIM), lambda h, part_ref: (0, 0, h))] * parts
        + [pl.BlockSpec((3, HEAD_DIM), lambda h, part_ref: (0, h))],
        scratch_shapes=[pltpu.VMEM((3, length, HEAD_DIM), jnp.bfloat16)],
    )
    return pl.pallas_call(
        functools.partial(grads_kernel, parts=parts),
        grid_spec=grid_spec,
        out_shape=[jax.ShapeDtypeStruct((3, rows, width), jnp.bfloat16)] * parts
        + [jax.ShapeDtypeStruct((3, width), jnp.float32)],
    )(part, positions, query_rows, key_rows, value_rows, grad_rows)


def per_device(queries, keys, values, grad_out, positions):
    query_rows = queries[0, 0]
    key_rows = keys[0, 0]
    value_rows = values[0, 0]
    grad_rows = grad_out[0, 0]
    token_positions = positions[0, 0].reshape(1, -1)
    length, columns = query_rows.shape
    sections = lax.axis_size("section")
    parts = lax.axis_size("mp")
    replicas = lax.axis_size("dp")
    part = lax.axis_index("mp")
    rows = length // parts
    head_count = columns // HEAD_DIM
    lead = max(1, head_count // 4)
    sizes = [lead, head_count - lead] if head_count > lead else [head_count]
    firsts = [sum(sizes[:c]) for c in range(len(sizes))]
    chunk_count = len(sizes)
    part_arg = jnp.reshape(part, (1,)).astype(jnp.int32)

    def pairs(shift):
        return [
            ((s + 1) * parts + m, s * parts + (m + shift) % parts)
            for s in range(sections - 1)
            for m in range(parts)
        ]

    arrived = [[None] * chunk_count for _ in range(parts)]
    sums = []
    for c in range(chunk_count):
        *grads, chunk_sums = chunk_grads(
            part_arg, token_positions, query_rows, key_rows, value_rows, grad_rows, firsts[c], sizes[c], parts
        )
        sums.append(chunk_sums)
        tie = []
        if c == chunk_count - 1:
            own = jnp.concatenate(sums, axis=1)
            relayed = lax.ppermute(own, "section", [(s + 1, s) for s in range(sections - 1)])
            tie.append(relayed)
        if c > 0:
            tie += [arrived[shift][c - 1] for shift in range(parts)]
        if tie:
            grads = lax.optimization_barrier((grads, tie))[0]
        for shift in range(parts):
            arrived[shift][c] = lax.ppermute(grads[shift], ("section", "mp"), pairs(shift))

    def receivers_sum(value, axis):
        count = lax.axis_size(axis)
        step = 1
        while step < count:
            ring = [(s * count + i, s * count + (i ^ step)) for s in range(sections - 1) for i in range(count)]
            value = value + lax.ppermute(value, ("section", axis), ring)
            step *= 2
        return value

    if chunk_count > 1:
        relayed = lax.optimization_barrier((relayed, arrived[0][-1]))[0]
    reduced = receivers_sum(relayed, "dp")
    slots = lax.dynamic_update_slice_in_dim(
        jnp.zeros((3, columns * parts), jnp.float32), reduced, part * columns, 1
    )
    totals = receivers_sum(slots, "mp")
    bias_grad = totals / math.sqrt(replicas * length)

    received = jnp.zeros((3, rows, columns * parts), jnp.bfloat16)
    for shift in range(parts):
        source = (part - shift) % parts
        for c in range(chunk_count):
            received = lax.dynamic_update_slice_in_dim(
                received, arrived[shift][c], source * columns + firsts[c] * HEAD_DIM, 2
            )
    return (received[None, None], bias_grad[None])


def solution(mesh):
    return jax.shard_map(
        per_device,
        mesh=mesh,
        in_specs=(
            P("section", "dp", None, "mp"),
            P("section", "dp", None, "mp"),
            P("section", "dp", None, "mp"),
            P("section", "dp", None, "mp"),
            P("section", "dp", None),
        ),
        out_specs=(P("section", "dp", None, "mp", None), P("section", None, None)),
        check_vma=False,
    )
```

```python
import functools
import math

import jax
import jax.numpy as jnp
from jax import lax
from jax.experimental import pallas as pl
from jax.experimental.pallas import tpu as pltpu
from jax.sharding import PartitionSpec as P

HEAD_DIM = 128
NT = (((1,), (1,)), ((), ()))


def grads_kernel(part_ref, pos_ref, q_ref, k_ref, v_ref, g_ref, *refs, parts):
    out_refs, sum_ref, full_ref = refs[:parts], refs[parts], refs[parts + 1]
    length = q_ref.shape[0]
    half = length // 2
    window = -(-half // 128) * 128
    rows = length // parts
    scaling = 1.0 / math.sqrt(HEAD_DIM)
    for b, lo in enumerate((0, length - window)):
        klo = b * half
        q = q_ref[lo : lo + window, :]
        g = g_ref[lo : lo + window, :]
        k = k_ref[klo : klo + half, :]
        v = v_ref[klo : klo + half, :]
        scores = lax.dot_general(k, q, NT, preferred_element_type=jnp.float32) * scaling
        kj = klo + lax.broadcasted_iota(jnp.int32, (half, window), 0)
        qi = lo + lax.broadcasted_iota(jnp.int32, (half, window), 1)
        start = lo + lax.broadcasted_iota(jnp.int32, (1, window), 1) - pos_ref[:, lo : lo + window]
        allowed = (kj <= qi) & (kj >= start)
        scores = jnp.where(allowed, scores, jnp.float32(-1e30))
        highest = jnp.max(scores, axis=0, keepdims=True)
        expont = jnp.exp(scores - highest)
        attn = expont / jnp.sum(expont, axis=0, keepdims=True)
        query = lo + lax.broadcasted_iota(jnp.int32, (1, window), 1)
        attn = jnp.where((query >= klo) & (query < klo + half), attn, jnp.float32(0.0))
        grad_v = jnp.dot(attn.astype(jnp.bfloat16), g, preferred_element_type=jnp.float32)
        grad_attn = lax.dot_general(v, g, NT, preferred_element_type=jnp.float32)
        delta = jnp.sum(attn * grad_attn, axis=0, keepdims=True)
        grad_scores = attn * (grad_attn - delta) * scaling
        grad_k = jnp.dot(grad_scores.astype(jnp.bfloat16), q, preferred_element_type=jnp.float32)
        grad_q = jnp.dot(grad_scores.T.astype(jnp.bfloat16), k, preferred_element_type=jnp.float32)
        keep = b * half - lo
        full_ref[0, b * half : (b + 1) * half, :] = grad_q[keep : keep + half].astype(jnp.bfloat16)
        full_ref[1, b * half : (b + 1) * half, :] = grad_k.astype(jnp.bfloat16)
        full_ref[2, b * half : (b + 1) * half, :] = grad_v.astype(jnp.bfloat16)
    sum_ref[...] = jnp.sum(full_ref[...].astype(jnp.float32), axis=1)
    part = part_ref[0]
    for shift, out_ref in enumerate(out_refs):
        target = (part + shift) % parts
        out_ref[...] = full_ref[:, pl.ds(pl.multiple_of(target * rows, 16), rows), :]


def chunk_grads(part, positions, query_rows, key_rows, value_rows, grad_rows, first, heads, parts):
    length = query_rows.shape[0]
    rows = length // parts
    width = heads * HEAD_DIM

    def column(h, part_ref):
        return (0, first + h)

    in_block = pl.BlockSpec((length, HEAD_DIM), column)
    grid_spec = pltpu.PrefetchScalarGridSpec(
        num_scalar_prefetch=1,
        grid=(heads,),
        in_specs=[pl.BlockSpec((1, length), lambda h, part_ref: (0, 0))] + [in_block] * 4,
        out_specs=[pl.BlockSpec((3, rows, HEAD_DIM), lambda h, part_ref: (0, 0, h))] * parts
        + [pl.BlockSpec((3, HEAD_DIM), lambda h, part_ref: (0, h))],
        scratch_shapes=[pltpu.VMEM((3, length, HEAD_DIM), jnp.bfloat16)],
    )
    return pl.pallas_call(
        functools.partial(grads_kernel, parts=parts),
        grid_spec=grid_spec,
        out_shape=[jax.ShapeDtypeStruct((3, rows, width), jnp.bfloat16)] * parts
        + [jax.ShapeDtypeStruct((3, width), jnp.float32)],
    )(part, positions, query_rows, key_rows, value_rows, grad_rows)


def per_device(queries, keys, values, grad_out, positions):
    query_rows = queries[0, 0]
    key_rows = keys[0, 0]
    value_rows = values[0, 0]
    grad_rows = grad_out[0, 0]
    token_positions = positions[0, 0].reshape(1, -1)
    length, columns = query_rows.shape
    sections = lax.axis_size("section")
    parts = lax.axis_size("mp")
    replicas = lax.axis_size("dp")
    part = lax.axis_index("mp")
    rows = length // parts
    head_count = columns // HEAD_DIM
    lead = max(1, head_count // 4)
    sizes = [lead, head_count - lead] if head_count > lead else [head_count]
    firsts = [sum(sizes[:c]) for c in range(len(sizes))]
    chunk_count = len(sizes)
    part_arg = jnp.reshape(part, (1,)).astype(jnp.int32)

    def pairs(shift):
        return [
            ((s + 1) * parts + m, s * parts + (m + shift) % parts)
            for s in range(sections - 1)
            for m in range(parts)
        ]

    arrived = [[None] * chunk_count for _ in range(parts)]
    sums = []
    for c in range(chunk_count):
        def run(*args, first=firsts[c], heads=sizes[c]):
            return tuple(chunk_grads(part_arg, *args, first, heads, parts))

        def skip(*args, heads=sizes[c]):
            width = heads * HEAD_DIM
            return tuple([jnp.zeros((3, rows, width), jnp.bfloat16)] * parts + [jnp.zeros((3, width), jnp.float32)])

        *grads, chunk_sums = lax.cond(
            lax.axis_index("section") > 0, run, skip, token_positions, query_rows, key_rows, value_rows, grad_rows
        )
        sums.append(chunk_sums)
        tie = []
        if c == chunk_count - 1:
            own = jnp.concatenate(sums, axis=1)
            relayed = lax.ppermute(own, "section", [(s + 1, s) for s in range(sections - 1)])
            tie.append(relayed)
        if c > 0:
            tie += [arrived[shift][c - 1] for shift in range(parts)]
        if tie:
            grads = lax.optimization_barrier((grads, tie))[0]
        for shift in range(parts):
            arrived[shift][c] = lax.ppermute(grads[shift], ("section", "mp"), pairs(shift))

    def receivers_sum(value, axis):
        count = lax.axis_size(axis)
        step = 1
        while step < count:
            ring = [(s * count + i, s * count + (i ^ step)) for s in range(sections - 1) for i in range(count)]
            value = value + lax.ppermute(value, ("section", axis), ring)
            step *= 2
        return value

    if chunk_count > 1:
        relayed = lax.optimization_barrier((relayed, arrived[0][-1]))[0]
    reduced = receivers_sum(relayed, "dp")
    slots = lax.dynamic_update_slice_in_dim(
        jnp.zeros((3, columns * parts), jnp.float32), reduced, part * columns, 1
    )
    totals = receivers_sum(slots, "mp")
    bias_grad = totals / math.sqrt(replicas * length)

    received = jnp.zeros((3, rows, columns * parts), jnp.bfloat16)
    for shift in range(parts):
        source = (part - shift) % parts
        for c in range(chunk_count):
            received = lax.dynamic_update_slice_in_dim(
                received, arrived[shift][c], source * columns + firsts[c] * HEAD_DIM, 2
            )
    return (received[None, None], bias_grad[None])


def solution(mesh):
    return jax.shard_map(
        per_device,
        mesh=mesh,
        in_specs=(
            P("section", "dp", None, "mp"),
            P("section", "dp", None, "mp"),
            P("section", "dp", None, "mp"),
            P("section", "dp", None, "mp"),
            P("section", "dp", None),
        ),
        out_specs=(P("section", "dp", None, "mp", None), P("section", None, None)),
        check_vma=False,
    )
```
